512 devices in a mesh: pairs: 128 (over y, z, core), tensor: 4 (over x).
Axes of the slice: x: 4, y: 8, z: 8, core: 2. Of those that a mesh axis runs over, the one named last changes fastest.
Arguments:
- queries: bfloat16 [32768, 4096], P('pairs', 'tensor'), may hold values from -100 to 100
- key_rows: bfloat16 [32768, 4096], P('pairs', 'tensor'), may hold values from -3.5 to 3.5
- value_rows: bfloat16 [32768, 4096], P('pairs', 'tensor'), may hold values from -12 to 12
- pair_ids: int32 [32768], P('pairs'), may hold values from 0 to 8, as said below
- out_weight: bfloat16 [4096, 4096], P('tensor', 'pairs'), may hold values from -0.09375 to 0.09375
- residual: bfloat16 [24576, 4096], P('pairs', 'tensor'), may hold values from -6 to 6
Outputs:
- hidden_out: bfloat16 [24576, 4096], P('pairs', 'tensor')
The draws below stay inside these ranges and needn't reach their ends.
Inputs may be any that keep to these rules, and one draw needn't show every extreme that they name: `pair_ids`: within each block of 256 rows the entries never fall; rows with a value below 8 come first and rows with value 8 form the block's tail; equal values below 8 form one pair. The used rows of blocks 2k and 2k + 1 together number at most 384, reached by some two blocks, and some block has no unused row.
All inputs are finite; a program needn't handle non-finite values.
Results may differ from the reference program's by a relative error of at most 0.0055.
Values may be sent and summed in bfloat16 or wider, within the bound.
No kernel may reach another device: no remote copies, remote signals or barrier semaphores. Data moves between devices by JAX's collectives and lax.ppermute only.
A program may use at most 64 MiB of HBM per device.

```python
import jax
import jax.numpy as jnp
from jax import lax

D = 4096
HEADS = 64
HEAD = 64
CAP = 256
SLOTS = 8
ROWS = 192
PADROWS = 32768
TOKENS = 24576
N_PAIRS = 128
N_TENSOR = 4


def paired_rows(key):
    full_width = HEADS * HEAD
    base_query = jnp.clip(jax.random.normal(jax.random.fold_in(key, 11), (PADROWS, full_width), jnp.float32), -8.0, 8.0) * 0.35
    base_key = jnp.clip(jax.random.normal(jax.random.fold_in(key, 12), (PADROWS, full_width), jnp.float32), -8.0, 8.0) * 0.35
    return (base_query, base_key)


def draw_queries(key, part):
    return paired_rows(key)[0].astype(jnp.bfloat16)


def draw_key_rows(key, part):
    return paired_rows(key)[1].astype(jnp.bfloat16)


def draw_pair_ids(key, part):
    devices = PADROWS // CAP
    pair_count = devices // 2
    first_live = jax.random.randint(jax.random.fold_in(key, 21), (pair_count,), 0, CAP + 1)
    raw_draw = jax.random.randint(jax.random.fold_in(key, 22), (pair_count,), 0, 1 << 20)
    room_left = jnp.minimum(CAP, 2 * ROWS - first_live)
    second_live = raw_draw % (room_left + 1)
    chosen = jax.random.randint(jax.random.fold_in(key, 23), (), 0, pair_count)
    picked = jnp.arange(pair_count) == chosen
    first_live = jnp.where(picked, CAP, first_live)
    second_live = jnp.where(picked, 2 * ROWS - CAP, second_live)
    flipped = jax.random.randint(jax.random.fold_in(key, 24), (pair_count,), 0, 2) == 1
    left_live = jnp.where(flipped, second_live, first_live)
    right_live = jnp.where(flipped, first_live, second_live)
    live_rows = jnp.stack([left_live, right_live], axis=1).reshape(devices)
    cut_points = jax.random.randint(jax.random.fold_in(key, 25), (devices, SLOTS - 1), 1, CAP)
    position = jnp.arange(CAP)
    counted = jnp.sum((cut_points[:, None, :] <= position[None, :, None]).astype(jnp.int32), axis=2)
    pair_index = jnp.where(position[None, :] < live_rows[:, None], counted, SLOTS)
    return pair_index.reshape(PADROWS).astype(jnp.int32)


def steps_of(stream_key, shape, cuts, least, high):
    factor_of = 1.0
    for dim, blocks in cuts:
        steps = jax.random.uniform(jax.random.fold_in(jax.random.fold_in(stream_key, 6), dim), (blocks,), jnp.float32, least / len(cuts), high / len(cuts))
        factor_of = factor_of * jnp.repeat(jnp.exp(steps), shape[dim] // blocks).reshape((-1,) + (1,) * (len(shape) - 1 - dim))
    return factor_of


def scatter_about(stream_key, extent, deviation, reach, cuts=(), kind=jnp.bfloat16):
    values = jax.random.normal(stream_key, extent, jnp.float32) * deviation
    if len(cuts) > 0:
        values = steps_of(stream_key, extent, cuts, -0.22, 0.18) * values
    return jnp.clip(values, min=-reach, max=reach).astype(kind)


def setup_inputs(seed: int = 0) -> dict:
    streams_of = jax.random.split(jax.random.key(seed), 7)
    queries = draw_queries(jax.random.fold_in(streams_of[6], 71), 0)
    key_rows = draw_key_rows(jax.random.fold_in(streams_of[6], 71), 0)
    value_rows = scatter_about(streams_of[2], (PADROWS, HEADS * HEAD), 2.0, 12.0, ((0, 128), (1, 4)))
    pair_ids = draw_pair_ids(jax.random.fold_in(streams_of[6], 71), 0)
    out_weight = scatter_about(streams_of[4], (HEADS * HEAD, D), (HEADS * HEAD) ** -0.5, 0.09375, ((0, 4), (1, 128)))
    residual = scatter_about(streams_of[5], (TOKENS, D), 1.0, 6.0, ((0, 128), (1, 4)))
    return {"queries": queries, "key_rows": key_rows, "value_rows": value_rows, "pair_ids": pair_ids, "out_weight": out_weight, "residual": residual}


def attend_block(block):
    query_block, key_block, value_block, id_block = block
    group_size = 8 if HEADS % 8 == 0 else HEADS

    def split_heads(stacked):
        return stacked.reshape(CAP, HEADS // group_size, group_size, HEAD).transpose(1, 0, 2, 3)

    allowed = (id_block[:, None] == id_block[None, :]) & (id_block[:, None] < SLOTS)

    def per_group(operands):
        query_part, key_part, value_part = operands
        scores = jnp.einsum("qhd,khd->hqk", query_part.astype(jnp.float32), key_part.astype(jnp.float32))
        masked = jnp.where(allowed[None], scores, -1e30)
        row_top = jnp.max(masked, axis=2, keepdims=True)
        exp_terms = jnp.where(allowed[None], jnp.exp(masked - row_top), 0.0)
        row_total = jnp.maximum(jnp.sum(exp_terms, axis=2, keepdims=True), 1.0)
        weights = lax.optimization_barrier((exp_terms / row_total).astype(jnp.bfloat16))
        mixed = jnp.einsum("hqk,khd->qhd", weights.astype(jnp.float32), value_part.astype(jnp.float32))
        return mixed.astype(jnp.bfloat16)

    grouped = lax.map(per_group, (split_heads(query_block), split_heads(key_block), split_heads(value_block)))
    return grouped.transpose(1, 0, 2, 3).reshape(CAP, HEADS * HEAD)


def reference(queries, key_rows, value_rows, pair_ids, out_weight, residual):
    full_width = HEADS * HEAD
    blocks = (queries.reshape(N_PAIRS, CAP, full_width), key_rows.reshape(N_PAIRS, CAP, full_width),
              value_rows.reshape(N_PAIRS, CAP, full_width), pair_ids.reshape(N_PAIRS, CAP))
    attended = lax.map(attend_block, blocks)
    id_blocks = pair_ids.reshape(N_PAIRS, CAP)
    live_count = jnp.sum((id_blocks < SLOTS).astype(jnp.int32), axis=1)
    row_start = jnp.cumsum(live_count).astype(jnp.int32) - live_count
    position = jnp.arange(CAP, dtype=jnp.int32)
    number = row_start[:, None] + position[None, :]
    target = jnp.where(position[None, :] < live_count[:, None],
                       (number % N_PAIRS) * ROWS + number // N_PAIRS, TOKENS).astype(jnp.int32)
    moved_attended = jnp.zeros((TOKENS, full_width), jnp.bfloat16).at[target.reshape(-1)].set(
        attended.reshape(-1, full_width), mode="drop")
    group_width = full_width // N_TENSOR
    projected = jnp.zeros((TOKENS, D), jnp.float32)
    for group_index in range(N_TENSOR):
        rows_part = moved_attended[:, group_index * group_width:(group_index + 1) * group_width]
        weight_part = out_weight[group_index * group_width:(group_index + 1) * group_width, :]
        partial_value = lax.optimization_barrier(
            jnp.dot(rows_part, weight_part, preferred_element_type=jnp.float32).astype(jnp.bfloat16))
        projected = projected + partial_value.astype(jnp.float32)
    projected = lax.optimization_barrier(projected.astype(jnp.bfloat16))
    return (residual.astype(jnp.float32) + projected.astype(jnp.float32)).astype(jnp.bfloat16)
```

```python
import jax
import jax.numpy as jnp
from jax import lax
from jax.sharding import PartitionSpec as P

HEAD = 64
SLOTS = 8


def carried_in(part, axis):
    place = lax.axis_index(axis)
    gathered = lax.all_gather(part, axis)
    earlier = jnp.arange(gathered.shape[0], dtype=jnp.int32) < place
    return jnp.sum(jnp.where(earlier, gathered, 0)), gathered


def attend_group(query_part, key_part, value_part, allowed):
    scores = jnp.einsum("qhd,khd->hqk", query_part, key_part, preferred_element_type=jnp.float32)
    masked = jnp.where(allowed[None], scores, -1e30)
    row_top = jnp.max(masked, axis=2, keepdims=True)
    exp_terms = jnp.where(allowed[None], jnp.exp(masked - row_top), 0.0)
    row_total = jnp.maximum(jnp.sum(exp_terms, axis=2, keepdims=True), 1.0)
    weights = (exp_terms / row_total).astype(jnp.bfloat16)
    mixed = jnp.einsum("hqk,khd->qhd", weights, value_part, preferred_element_type=jnp.float32)
    return mixed.astype(jnp.bfloat16)


def shards(queries, key_rows, value_rows, pair_ids, out_weight, residual):
    cap_rows = queries.shape[0]
    local_width = queries.shape[1]
    heads_local = local_width // HEAD
    group_size = 4
    balanced_rows = residual.shape[0]
    allowed = (pair_ids[:, None] == pair_ids[None, :]) & (pair_ids[:, None] < SLOTS)

    def split_heads(stacked):
        return stacked.reshape(cap_rows, heads_local // group_size, group_size, HEAD).transpose(
            1, 0, 2, 3
        )

    def per_group(operands):
        return attend_group(operands[0], operands[1], operands[2], allowed)

    grouped = lax.map(
        per_group, (split_heads(queries), split_heads(key_rows), split_heads(value_rows))
    )
    attended = grouped.transpose(1, 0, 2, 3).reshape(cap_rows, local_width)
    live_rows = jnp.sum((pair_ids < SLOTS).astype(jnp.int32))
    devices = lax.axis_size("pairs")
    row_start, all_live = carried_in(live_rows, "pairs")
    all_start = jnp.cumsum(all_live) - all_live
    partial_value = jnp.dot(
        attended,
        lax.all_gather(out_weight, "pairs", axis=1, tiled=True),
        preferred_element_type=jnp.float32,
    )
    payload = lax.psum_scatter(
        partial_value.astype(jnp.bfloat16), "tensor", scatter_dimension=1, tiled=True
    )
    per_peer = cap_rows // devices
    feature_width = payload.shape[1]
    peer_index = jnp.arange(devices, dtype=jnp.int32)
    turn_index = jnp.arange(per_peer, dtype=jnp.int32)
    source_rows = ((peer_index - row_start) % devices)[:, None] + devices * turn_index[None, :]
    outgoing = jnp.take(payload, source_rows.reshape(-1), axis=0).reshape(
        devices, per_peer, feature_width
    )
    incoming = lax.all_to_all(outgoing, "pairs", split_axis=0, concat_axis=0, tiled=True)
    me = lax.axis_index("pairs")
    peer_rows = ((me - all_start) % devices)[:, None] + devices * turn_index[None, :]
    incoming_slots = jnp.where(
        peer_rows < all_live[:, None], (all_start[:, None] + peer_rows) // devices, balanced_rows
    ).astype(jnp.int32)
    landed = jnp.zeros((balanced_rows, feature_width), payload.dtype)
    moved_rows = landed.at[incoming_slots.reshape(-1)].set(
        incoming.reshape(-1, feature_width), mode="drop"
    )
    return (residual.astype(jnp.float32) + moved_rows.astype(jnp.float32)).astype(jnp.bfloat16)


def solution(mesh):
    in_specs = (
        P("pairs", "tensor"),
        P("pairs", "tensor"),
        P("pairs", "tensor"),
        P("pairs"),
        P("tensor", "pairs"),
        P("pairs", "tensor"),
    )
    out_specs = P("pairs", "tensor")
    return jax.shard_map(shards, mesh=mesh, in_specs=in_specs, out_specs=out_specs, check_vma=False)
```

```python
import jax
import jax.numpy as jnp
from jax import lax
from jax.sharding import PartitionSpec as P

HEAD = 64
SLOTS = 8


def carried_in(part, axis):
    place = lax.axis_index(axis)
    gathered = lax.all_gather(part, axis)
    earlier = jnp.arange(gathered.shape[0], dtype=jnp.int32) < place
    return jnp.sum(jnp.where(earlier, gathered, 0)), gathered


def attend_group(query_part, key_part, value_part, allowed):
    scores = jnp.einsum("qhd,khd->hqk", query_part, key_part, preferred_element_type=jnp.float32)
    masked = jnp.where(allowed[None], scores, -1e30)
    row_top = jnp.max(masked, axis=2, keepdims=True)
    exp_terms = jnp.where(allowed[None], jnp.exp(masked - row_top), 0.0)
    row_total = jnp.maximum(jnp.sum(exp_terms, axis=2, keepdims=True), 1.0)
    weights = (exp_terms / row_total).astype(jnp.bfloat16)
    mixed = jnp.einsum("hqk,khd->qhd", weights, value_part, preferred_element_type=jnp.float32)
    return mixed.astype(jnp.bfloat16)


def shards(queries, key_rows, value_rows, pair_ids, out_weight, residual):
    cap_rows = queries.shape[0]
    local_width = queries.shape[1]
    heads_local = local_width // HEAD
    group_size = 4
    balanced_rows = residual.shape[0]
    allowed = (pair_ids[:, None] == pair_ids[None, :]) & (pair_ids[:, None] < SLOTS)

    def split_heads(stacked):
        return stacked.reshape(cap_rows, heads_local // group_size, group_size, HEAD).transpose(
            1, 0, 2, 3
        )

    def per_group(operands):
        return attend_group(operands[0], operands[1], operands[2], allowed)

    grouped = lax.map(
        per_group, (split_heads(queries), split_heads(key_rows), split_heads(value_rows))
    )
    attended = grouped.transpose(1, 0, 2, 3).reshape(cap_rows, local_width)
    live_rows = jnp.sum((pair_ids < SLOTS).astype(jnp.int32))
    devices = lax.axis_size("pairs")
    row_start, all_live = carried_in(live_rows, "pairs")
    all_start = jnp.cumsum(all_live) - all_live
    per_peer = cap_rows // devices
    peer_index = jnp.arange(devices, dtype=jnp.int32)
    turn_index = jnp.arange(per_peer, dtype=jnp.int32)
    source_rows = ((peer_index - row_start) % devices)[:, None] + devices * turn_index[None, :]
    outgoing = jnp.take(attended, source_rows.reshape(-1), axis=0).reshape(
        devices, per_peer, local_width
    )
    incoming = lax.all_to_all(outgoing, "pairs", split_axis=0, concat_axis=0, tiled=True)
    me = lax.axis_index("pairs")
    peer_rows = ((me - all_start) % devices)[:, None] + devices * turn_index[None, :]
    incoming_slots = jnp.where(
        peer_rows < all_live[:, None], (all_start[:, None] + peer_rows) // devices, balanced_rows
    ).astype(jnp.int32)
    landed = jnp.zeros((balanced_rows, local_width), attended.dtype)
    moved_rows = landed.at[incoming_slots.reshape(-1)].set(
        incoming.reshape(-1, local_width), mode="drop"
    )
    partial_value = jnp.dot(
        moved_rows,
        lax.all_gather(out_weight, "pairs", axis=1, tiled=True),
        preferred_element_type=jnp.float32,
    )
    payload = lax.psum_scatter(
        partial_value.astype(jnp.bfloat16), "tensor", scatter_dimension=1, tiled=True
    )
    return (residual.astype(jnp.float32) + payload.astype(jnp.float32)).astype(jnp.bfloat16)


def solution(mesh):
    in_specs = (
        P("pairs", "tensor"),
        P("pairs", "tensor"),
        P("pairs", "tensor"),
        P("pairs"),
        P("tensor", "pairs"),
        P("pairs", "tensor"),
    )
    out_specs = P("pairs", "tensor")
    return jax.shard_map(shards, mesh=mesh, in_specs=in_specs, out_specs=out_specs, check_vma=False)
```

```python
import jax
import jax.numpy as jnp
from jax import lax
from jax.sharding import PartitionSpec as P

HEAD = 64
SLOTS = 8


def carried_in(part, axis):
    place = lax.axis_index(axis[0]) * lax.axis_size(axis[1]) + lax.axis_index(axis[1])
    gathered = lax.all_gather(part, axis)
    earlier = jnp.arange(gathered.shape[0], dtype=jnp.int32) < place
    return jnp.sum(jnp.where(earlier, gathered, 0)), gathered


def attend_group(query_part, key_part, value_part, allowed):
    scores = jnp.einsum("qhd,khd->hqk", query_part, key_part, preferred_element_type=jnp.float32)
    masked = jnp.where(allowed[None], scores, -1e30)
    row_top = jnp.max(masked, axis=2, keepdims=True)
    exp_terms = jnp.where(allowed[None], jnp.exp(masked - row_top), 0.0)
    row_total = jnp.maximum(jnp.sum(exp_terms, axis=2, keepdims=True), 1.0)
    weights = (exp_terms / row_total).astype(jnp.bfloat16)
    mixed = jnp.einsum("hqk,khd->qhd", weights, value_part, preferred_element_type=jnp.float32)
    return mixed.astype(jnp.bfloat16)


def shards(queries, key_rows, value_rows, pair_ids, out_weight, residual):
    cap_rows = queries.shape[0]
    local_width = queries.shape[1]
    heads_local = local_width // HEAD
    group_size = 4
    balanced_rows = residual.shape[0]
    allowed = (pair_ids[:, None] == pair_ids[None, :]) & (pair_ids[:, None] < SLOTS)

    def split_heads(stacked):
        return stacked.reshape(cap_rows, heads_local // group_size, group_size, HEAD).transpose(
            1, 0, 2, 3
        )

    def per_group(operands):
        return attend_group(operands[0], operands[1], operands[2], allowed)

    grouped = lax.map(
        per_group, (split_heads(queries), split_heads(key_rows), split_heads(value_rows))
    )
    attended = grouped.transpose(1, 0, 2, 3).reshape(cap_rows, local_width)
    live_rows = jnp.sum((pair_ids < SLOTS).astype(jnp.int32))
    devices = lax.axis_size("chip") * lax.axis_size("core")
    row_start, all_live = carried_in(live_rows, ("chip", "core"))
    all_start = jnp.cumsum(all_live) - all_live
    per_peer = cap_rows // devices
    peer_index = jnp.arange(devices, dtype=jnp.int32)
    turn_index = jnp.arange(per_peer, dtype=jnp.int32)
    source_rows = ((peer_index - row_start) % devices)[:, None] + devices * turn_index[None, :]
    outgoing = jnp.take(attended, source_rows.reshape(-1), axis=0).reshape(
        devices, per_peer, local_width
    )
    incoming = lax.all_to_all(outgoing, ("chip", "core"), split_axis=0, concat_axis=0, tiled=True)
    me = lax.axis_index("chip") * lax.axis_size("core") + lax.axis_index("core")
    peer_rows = ((me - all_start) % devices)[:, None] + devices * turn_index[None, :]
    incoming_slots = jnp.where(
        peer_rows < all_live[:, None], (all_start[:, None] + peer_rows) // devices, balanced_rows
    ).astype(jnp.int32)
    landed = jnp.zeros((balanced_rows, local_width), attended.dtype)
    moved_rows = landed.at[incoming_slots.reshape(-1)].set(
        incoming.reshape(-1, local_width), mode="drop"
    )
    cores = lax.axis_size("core")
    chips = devices // cores
    stripe = out_weight.shape[1]
    same_core = lax.all_gather(out_weight, "chip", axis=1, tiled=True)
    both_cores = lax.all_gather(same_core, "core")
    partial_value = jnp.einsum(
        "rk,ckmj->rmcj",
        moved_rows,
        both_cores.reshape(cores, -1, chips, stripe),
        preferred_element_type=jnp.float32,
    ).astype(jnp.bfloat16)
    payload = lax.psum_scatter(
        partial_value.reshape(balanced_rows, -1), "tensor", scatter_dimension=1, tiled=True
    )
    return (residual.astype(jnp.float32) + payload.astype(jnp.float32)).astype(jnp.bfloat16)


def solution(mesh):
    pairs_size, tensor_size = mesh.devices.shape
    split_mesh = jax.sharding.Mesh(
        mesh.devices.reshape(pairs_size // 2, 2, tensor_size), ("chip", "core", "tensor")
    )
    rows = ("chip", "core")
    in_specs = (
        P(rows, "tensor"),
        P(rows, "tensor"),
        P(rows, "tensor"),
        P(rows),
        P("tensor", rows),
        P(rows, "tensor"),
    )
    out_specs = P(rows, "tensor")
    return jax.shard_map(
        shards, mesh=split_mesh, in_specs=in_specs, out_specs=out_specs, check_vma=False
    )
```

```python
import jax
import jax.numpy as jnp
from jax import lax
from jax.sharding import PartitionSpec as P

HEAD = 64
SLOTS = 8


def carried_in(part, axis):
    place = lax.axis_index(axis)
    gathered = lax.all_gather(part, axis)
    earlier = jnp.arange(gathered.shape[0], dtype=jnp.int32) < place
    return jnp.sum(jnp.where(earlier, gathered, 0)), gathered


def attend_group(query_part, key_part, value_part, allowed):
    scores = jnp.einsum("qhd,khd->hqk", query_part, key_part, preferred_element_type=jnp.float32)
    masked = jnp.where(allowed[None], scores, -1e30)
    row_top = jnp.max(masked, axis=2, keepdims=True)
    exp_terms = jnp.where(allowed[None], jnp.exp(masked - row_top), 0.0)
    row_total = jnp.maximum(jnp.sum(exp_terms, axis=2, keepdims=True), 1.0)
    weights = (exp_terms / row_total).astype(jnp.bfloat16)
    mixed = jnp.einsum("hqk,khd->qhd", weights, value_part, preferred_element_type=jnp.float32)
    return mixed.astype(jnp.bfloat16)


def shards(queries, key_rows, value_rows, pair_ids, out_weight, residual):
    cap_rows = queries.shape[0]
    local_width = queries.shape[1]
    heads_local = local_width // HEAD
    group_size = 4
    balanced_rows = residual.shape[0]
    allowed = (pair_ids[:, None] == pair_ids[None, :]) & (pair_ids[:, None] < SLOTS)

    def split_heads(stacked):
        return stacked.reshape(cap_rows, heads_local // group_size, group_size, HEAD).transpose(
            1, 0, 2, 3
        )

    def per_group(operands):
        return attend_group(operands[0], operands[1], operands[2], allowed)

    grouped = lax.map(
        per_group, (split_heads(queries), split_heads(key_rows), split_heads(value_rows))
    )
    attended = grouped.transpose(1, 0, 2, 3).reshape(cap_rows, local_width)
    live_rows = jnp.sum((pair_ids < SLOTS).astype(jnp.int32))
    devices = lax.axis_size("pairs")
    row_start, all_live = carried_in(live_rows, "pairs")
    all_start = jnp.cumsum(all_live) - all_live
    per_peer = cap_rows // devices
    peer_index = jnp.arange(devices, dtype=jnp.int32)
    turn_index = jnp.arange(per_peer, dtype=jnp.int32)
    source_rows = ((peer_index - row_start) % devices)[:, None] + devices * turn_index[None, :]
    outgoing = jnp.take(attended, source_rows.reshape(-1), axis=0).reshape(
        devices, per_peer, local_width
    )
    incoming = lax.all_to_all(outgoing, "pairs", split_axis=0, concat_axis=0, tiled=True)
    me = lax.axis_index("pairs")
    peer_rows = ((me - all_start) % devices)[:, None] + devices * turn_index[None, :]
    incoming_slots = jnp.where(
        peer_rows < all_live[:, None], (all_start[:, None] + peer_rows) // devices, balanced_rows
    ).astype(jnp.int32)
    landed = jnp.zeros((balanced_rows, local_width), attended.dtype)
    moved_rows = landed.at[incoming_slots.reshape(-1)].set(
        incoming.reshape(-1, local_width), mode="drop"
    )
    partial_value = jnp.dot(
        moved_rows,
        lax.all_gather(out_weight, "pairs", axis=1, tiled=True),
        preferred_element_type=jnp.float32,
    )
    tensor_parts = lax.axis_size("tensor")
    by_group = (
        partial_value.astype(jnp.bfloat16)
        .reshape(balanced_rows, tensor_parts, local_width)
        .transpose(1, 0, 2)
    )
    received = lax.all_to_all(by_group, "tensor", 0, 0, tiled=True)
    projected = jnp.sum(received.astype(jnp.float32), axis=0).astype(jnp.bfloat16)
    return (residual.astype(jnp.float32) + projected.astype(jnp.float32)).astype(jnp.bfloat16)


def solution(mesh):
    in_specs = (
        P("pairs", "tensor"),
        P("pairs", "tensor"),
        P("pairs", "tensor"),
        P("pairs"),
        P("tensor", "pairs"),
        P("pairs", "tensor"),
    )
    out_specs = P("pairs", "tensor")
    return jax.shard_map(shards, mesh=mesh, in_specs=in_specs, out_specs=out_specs, check_vma=False)
```

```python
import jax
import jax.numpy as jnp
from jax import lax
from jax.sharding import PartitionSpec as P

HEAD = 64
SLOTS = 8


def carried_in(part, axis):
    place = lax.axis_index(axis)
    gathered = lax.all_gather(part, axis)
    earlier = jnp.arange(gathered.shape[0], dtype=jnp.int32) < place
    return jnp.sum(jnp.where(earlier, gathered, 0)), gathered


def attend_group(query_part, key_part, value_part, allowed):
    scores = jnp.einsum("qhd,khd->hqk", query_part, key_part, preferred_element_type=jnp.float32)
    masked = jnp.where(allowed[None], scores, -1e30)
    row_top = jnp.max(masked, axis=2, keepdims=True)
    exp_terms = jnp.where(allowed[None], jnp.exp(masked - row_top), 0.0)
    row_total = jnp.maximum(jnp.sum(exp_terms, axis=2, keepdims=True), 1.0)
    weights = (exp_terms / row_total).astype(jnp.bfloat16)
    mixed = jnp.einsum("hqk,khd->qhd", weights, value_part, preferred_element_type=jnp.float32)
    return mixed.astype(jnp.bfloat16)


def shards(queries, key_rows, value_rows, pair_ids, out_weight, residual):
    cap_rows = queries.shape[0]
    local_width = queries.shape[1]
    heads_local = local_width // HEAD
    group_size = 4
    balanced_rows = residual.shape[0]
    allowed = (pair_ids[:, None] == pair_ids[None, :]) & (pair_ids[:, None] < SLOTS)

    def split_heads(stacked):
        return stacked.reshape(cap_rows, heads_local // group_size, group_size, HEAD).transpose(
            1, 0, 2, 3
        )

    def per_group(operands):
        return attend_group(operands[0], operands[1], operands[2], allowed)

    grouped = lax.map(
        per_group, (split_heads(queries), split_heads(key_rows), split_heads(value_rows))
    )
    attended = grouped.transpose(1, 0, 2, 3).reshape(cap_rows, local_width)
    live_rows = jnp.sum((pair_ids < SLOTS).astype(jnp.int32))
    devices = lax.axis_size("pairs")
    row_start, all_live = carried_in(live_rows, "pairs")
    all_start = jnp.cumsum(all_live) - all_live
    per_peer = cap_rows // devices
    peer_index = jnp.arange(devices, dtype=jnp.int32)
    turn_index = jnp.arange(per_peer, dtype=jnp.int32)
    source_rows = ((peer_index - row_start) % devices)[:, None] + devices * turn_index[None, :]
    outgoing = jnp.take(attended, source_rows.reshape(-1), axis=0).reshape(
        devices, per_peer, local_width
    )
    incoming = lax.all_to_all(outgoing, "pairs", split_axis=0, concat_axis=0, tiled=True)
    me = lax.axis_index("pairs")
    peer_rows = ((me - all_start) % devices)[:, None] + devices * turn_index[None, :]
    incoming_slots = jnp.where(
        peer_rows < all_live[:, None], (all_start[:, None] + peer_rows) // devices, balanced_rows
    ).astype(jnp.int32)
    landed = jnp.zeros((balanced_rows, local_width), attended.dtype)
    moved_rows = landed.at[incoming_slots.reshape(-1)].set(
        incoming.reshape(-1, local_width), mode="drop"
    )
    tensor_parts = lax.axis_size("tensor")
    group_width = out_weight.shape[1] // tensor_parts
    feature_stripes = devices // tensor_parts
    tensor_place = lax.axis_index("tensor")
    pieces = out_weight.reshape(local_width, tensor_parts, group_width)
    dealt = []
    for turn in range(tensor_parts):
        pairing = []
        for stripe_owner in range(devices):
            for block in range(tensor_parts):
                piece = (block + turn) % tensor_parts
                target = tensor_parts * (stripe_owner % feature_stripes) + piece
                pairing.append(
                    (stripe_owner * tensor_parts + block,
                     target * tensor_parts + stripe_owner // feature_stripes)
                )
        sent = jnp.take(pieces, (tensor_place + turn) % tensor_parts, axis=1)
        dealt.append(lax.ppermute(sent, ("pairs", "tensor"), pairing))
    piece_here = me % tensor_parts
    order = (piece_here - jnp.arange(tensor_parts, dtype=jnp.int32)) % tensor_parts
    own_columns = jnp.take(jnp.stack(dealt), order, axis=0).reshape(-1, group_width)
    group_weight_t = lax.all_gather(own_columns.T, "pairs", axis=0, tiled=True)
    spread = jnp.broadcast_to(moved_rows[None], (tensor_parts,) + moved_rows.shape)
    all_groups = lax.all_to_all(spread, "tensor", 0, 0, tiled=True)
    projected = jnp.zeros(moved_rows.shape, jnp.float32)
    for group in range(tensor_parts):
        partial_value = lax.dot_general(
            all_groups[group],
            group_weight_t[:, group * local_width:(group + 1) * local_width],
            (((1,), (1,)), ((), ())),
            preferred_element_type=jnp.float32,
        )
        projected = projected + partial_value.astype(jnp.bfloat16).astype(jnp.float32)
    projected = projected.astype(jnp.bfloat16)
    return (residual.astype(jnp.float32) + projected.astype(jnp.float32)).astype(jnp.bfloat16)


def solution(mesh):
    in_specs = (
        P("pairs", "tensor"),
        P("pairs", "tensor"),
        P("pairs", "tensor"),
        P("pairs"),
        P("tensor", "pairs"),
        P("pairs", "tensor"),
    )
    out_specs = P("pairs", "tensor")
    return jax.shard_map(shards, mesh=mesh, in_specs=in_specs, out_specs=out_specs, check_vma=False)
```

```python
import jax
import jax.numpy as jnp
from jax import lax
from jax.sharding import PartitionSpec as P

HEAD = 64
SLOTS = 8


def carried_in(part, axis):
    place = lax.axis_index(axis)
    gathered = lax.all_gather(part, axis)
    earlier = jnp.arange(gathered.shape[0], dtype=jnp.int32) < place
    return jnp.sum(jnp.where(earlier, gathered, 0)), gathered


def attend_group(query_part, key_part, value_part, allowed):
    scores = jnp.einsum("qhd,khd->hqk", query_part, key_part, preferred_element_type=jnp.float32)
    masked = jnp.where(allowed[None], scores, -1e30)
    row_top = jnp.max(masked, axis=2, keepdims=True)
    exp_terms = jnp.where(allowed[None], jnp.exp(masked - row_top), 0.0)
    row_total = jnp.maximum(jnp.sum(exp_terms, axis=2, keepdims=True), 1.0)
    weights = (exp_terms / row_total).astype(jnp.bfloat16)
    mixed = jnp.einsum("hqk,khd->qhd", weights, value_part, preferred_element_type=jnp.float32)
    return mixed.astype(jnp.bfloat16)


def shards(queries, key_rows, value_rows, pair_ids, out_weight, residual):
    cap_rows = queries.shape[0]
    local_width = queries.shape[1]
    heads_local = local_width // HEAD
    group_size = 4
    balanced_rows = residual.shape[0]
    allowed = (pair_ids[:, None] == pair_ids[None, :]) & (pair_ids[:, None] < SLOTS)

    def split_heads(stacked):
        return stacked.reshape(cap_rows, heads_local // group_size, group_size, HEAD).transpose(
            1, 0, 2, 3
        )

    def per_group(operands):
        return attend_group(operands[0], operands[1], operands[2], allowed)

    grouped = lax.map(
        per_group, (split_heads(queries), split_heads(key_rows), split_heads(value_rows))
    )
    attended = grouped.transpose(1, 0, 2, 3).reshape(cap_rows, local_width)
    live_rows = jnp.sum((pair_ids < SLOTS).astype(jnp.int32))
    devices = lax.axis_size("pairs")
    row_start, all_live = carried_in(live_rows, "pairs")
    all_start = jnp.cumsum(all_live) - all_live
    per_peer = cap_rows // devices
    peer_index = jnp.arange(devices, dtype=jnp.int32)
    turn_index = jnp.arange(per_peer, dtype=jnp.int32)
    source_rows = ((peer_index - row_start) % devices)[:, None] + devices * turn_index[None, :]
    outgoing = jnp.take(attended, source_rows.reshape(-1), axis=0).reshape(
        devices, per_peer, local_width
    )
    incoming = lax.all_to_all(outgoing, "pairs", split_axis=0, concat_axis=0, tiled=True)
    me = lax.axis_index("pairs")
    peer_rows = ((me - all_start) % devices)[:, None] + devices * turn_index[None, :]
    incoming_slots = jnp.where(
        peer_rows < all_live[:, None], (all_start[:, None] + peer_rows) // devices, balanced_rows
    ).astype(jnp.int32)
    landed = jnp.zeros((balanced_rows, local_width), attended.dtype)
    moved_rows = landed.at[incoming_slots.reshape(-1)].set(
        incoming.reshape(-1, local_width), mode="drop"
    )
    group_weight = lax.all_gather(out_weight, "pairs", axis=1, tiled=True)
    tensor_parts = lax.axis_size("tensor")
    tensor_place = lax.axis_index("tensor")

    def group_product(group):
        columns = lax.dynamic_slice_in_dim(group_weight, group * local_width, local_width, 1)
        return jnp.dot(moved_rows, columns, preferred_element_type=jnp.float32).astype(jnp.bfloat16)

    arrived = []
    for shift in range(1, tensor_parts):
        sent = group_product((tensor_place + shift) % tensor_parts)
        pairing = [(i, (i + shift) % tensor_parts) for i in range(tensor_parts)]
        arrived.append(lax.ppermute(sent, "tensor", pairing))
    total = group_product(tensor_place).astype(jnp.float32)
    for part in arrived:
        total = total + part.astype(jnp.float32)
    projected = total.astype(jnp.bfloat16)
    return (residual.astype(jnp.float32) + projected.astype(jnp.float32)).astype(jnp.bfloat16)


def solution(mesh):
    in_specs = (
        P("pairs", "tensor"),
        P("pairs", "tensor"),
        P("pairs", "tensor"),
        P("pairs"),
        P("tensor", "pairs"),
        P("pairs", "tensor"),
    )
    out_specs = P("pairs", "tensor")
    return jax.shard_map(shards, mesh=mesh, in_specs=in_specs, out_specs=out_specs, check_vma=False)
```

```python
import jax
import jax.numpy as jnp
from jax import lax
from jax.sharding import PartitionSpec as P

HEAD = 64
SLOTS = 8


def carried_in(part, axis):
    place = lax.axis_index(axis)
    gathered = lax.all_gather(part, axis)
    earlier = jnp.arange(gathered.shape[0], dtype=jnp.int32) < place
    return jnp.sum(jnp.where(earlier, gathered, 0)), gathered


def attend_group(query_part, key_part, value_part, allowed):
    scores = jnp.einsum("qhd,khd->hqk", query_part, key_part, preferred_element_type=jnp.float32)
    masked = jnp.where(allowed[None], scores, -1e30)
    row_top = jnp.max(masked, axis=2, keepdims=True)
    exp_terms = jnp.where(allowed[None], jnp.exp(masked - row_top), 0.0)
    row_total = jnp.maximum(jnp.sum(exp_terms, axis=2, keepdims=True), 1.0)
    weights = (exp_terms / row_total).astype(jnp.bfloat16)
    mixed = jnp.einsum("hqk,khd->qhd", weights, value_part, preferred_element_type=jnp.float32)
    return mixed.astype(jnp.bfloat16)


def shards(queries, key_rows, value_rows, pair_ids, out_weight, residual):
    cap_rows = queries.shape[0]
    local_width = queries.shape[1]
    heads_local = local_width // HEAD
    group_size = 4
    balanced_rows = residual.shape[0]
    allowed = (pair_ids[:, None] == pair_ids[None, :]) & (pair_ids[:, None] < SLOTS)

    def split_heads(stacked):
        return stacked.reshape(cap_rows, heads_local // group_size, group_size, HEAD).transpose(
            1, 0, 2, 3
        )

    def per_group(operands):
        return attend_group(operands[0], operands[1], operands[2], allowed)

    grouped = lax.map(
        per_group, (split_heads(queries), split_heads(key_rows), split_heads(value_rows))
    )
    attended = grouped.transpose(1, 0, 2, 3).reshape(cap_rows, local_width)
    live_rows = jnp.sum((pair_ids < SLOTS).astype(jnp.int32))
    devices = lax.axis_size("pairs")
    row_start, all_live = carried_in(live_rows, "pairs")
    all_start = jnp.cumsum(all_live) - all_live
    per_peer = cap_rows // devices
    peer_index = jnp.arange(devices, dtype=jnp.int32)
    turn_index = jnp.arange(per_peer, dtype=jnp.int32)
    source_rows = ((peer_index - row_start) % devices)[:, None] + devices * turn_index[None, :]
    outgoing = jnp.take(attended, source_rows.reshape(-1), axis=0).reshape(
        devices, per_peer, local_width
    )
    incoming = lax.all_to_all(outgoing, "pairs", split_axis=0, concat_axis=0, tiled=True)
    me = lax.axis_index("pairs")
    peer_rows = ((me - all_start) % devices)[:, None] + devices * turn_index[None, :]
    incoming_slots = jnp.where(
        peer_rows < all_live[:, None], (all_start[:, None] + peer_rows) // devices, balanced_rows
    ).astype(jnp.int32)
    landed = jnp.zeros((balanced_rows, local_width), attended.dtype)
    moved_rows = landed.at[incoming_slots.reshape(-1)].set(
        incoming.reshape(-1, local_width), mode="drop"
    )
    tensor_parts = lax.axis_size("tensor")
    half = local_width // 2
    group_weight = lax.all_gather(out_weight, "pairs", axis=1, tiled=True).reshape(
        local_width, tensor_parts, 2, half
    )
    first = jnp.einsum(
        "rk,kgn->rgn", moved_rows, group_weight[:, :, 0], preferred_element_type=jnp.float32
    ).astype(jnp.bfloat16)
    summed_first = lax.psum_scatter(
        first.reshape(balanced_rows, -1), "tensor", scatter_dimension=1, tiled=True
    )
    second = jnp.einsum(
        "rk,kgn->grn", moved_rows, group_weight[:, :, 1], preferred_element_type=jnp.float32
    ).astype(jnp.bfloat16)
    received = lax.all_to_all(second, "tensor", 0, 0, tiled=True)
    summed_second = jnp.sum(received.astype(jnp.float32), axis=0).astype(jnp.bfloat16)
    projected = jnp.concatenate([summed_first, summed_second], axis=1)
    return (residual.astype(jnp.float32) + projected.astype(jnp.float32)).astype(jnp.bfloat16)


def solution(mesh):
    in_specs = (
        P("pairs", "tensor"),
        P("pairs", "tensor"),
        P("pairs", "tensor"),
        P("pairs"),
        P("tensor", "pairs"),
        P("pairs", "tensor"),
    )
    out_specs = P("pairs", "tensor")
    return jax.shard_map(shards, mesh=mesh, in_specs=in_specs, out_specs=out_specs, check_vma=False)
```

```python
import jax
import jax.numpy as jnp
from jax import lax
from jax.sharding import PartitionSpec as P

HEAD = 64
SLOTS = 8


def carried_in(part, axis):
    place = lax.axis_index(axis)
    gathered = lax.all_gather(part, axis)
    earlier = jnp.arange(gathered.shape[0], dtype=jnp.int32) < place
    return jnp.sum(jnp.where(earlier, gathered, 0)), gathered


def attend_group(query_part, key_part, value_part, allowed):
    scores = jnp.einsum("qhd,khd->hqk", query_part, key_part, preferred_element_type=jnp.float32)
    masked = jnp.where(allowed[None], scores, -1e30)
    row_top = jnp.max(masked, axis=2, keepdims=True)
    exp_terms = jnp.where(allowed[None], jnp.exp(masked - row_top), 0.0)
    row_total = jnp.maximum(jnp.sum(exp_terms, axis=2, keepdims=True), 1.0)
    weights = (exp_terms / row_total).astype(jnp.bfloat16)
    mixed = jnp.einsum("hqk,khd->qhd", weights, value_part, preferred_element_type=jnp.float32)
    return mixed.astype(jnp.bfloat16)


def shards(queries, key_rows, value_rows, pair_ids, out_weight, residual):
    cap_rows = queries.shape[0]
    local_width = queries.shape[1]
    heads_local = local_width // HEAD
    group_size = 4
    balanced_rows = residual.shape[0]
    allowed = (pair_ids[:, None] == pair_ids[None, :]) & (pair_ids[:, None] < SLOTS)

    def split_heads(stacked):
        return stacked.reshape(cap_rows, heads_local // group_size, group_size, HEAD).transpose(
            1, 0, 2, 3
        )

    def per_group(operands):
        return attend_group(operands[0], operands[1], operands[2], allowed)

    grouped = lax.map(
        per_group, (split_heads(queries), split_heads(key_rows), split_heads(value_rows))
    )
    attended = grouped.transpose(1, 0, 2, 3).reshape(cap_rows, local_width)
    live_rows = jnp.sum((pair_ids < SLOTS).astype(jnp.int32))
    devices = lax.axis_size("pairs")
    row_start, all_live = carried_in(live_rows, "pairs")
    all_start = jnp.cumsum(all_live) - all_live
    per_peer = cap_rows // devices
    peer_index = jnp.arange(devices, dtype=jnp.int32)
    turn_index = jnp.arange(per_peer, dtype=jnp.int32)
    source_rows = ((peer_index - row_start) % devices)[:, None] + devices * turn_index[None, :]
    outgoing = jnp.take(attended, source_rows.reshape(-1), axis=0).reshape(
        devices, per_peer, local_width
    )
    incoming = lax.all_to_all(outgoing, "pairs", split_axis=0, concat_axis=0, tiled=True)
    me = lax.axis_index("pairs")
    peer_rows = ((me - all_start) % devices)[:, None] + devices * turn_index[None, :]
    incoming_slots = jnp.where(
        peer_rows < all_live[:, None], (all_start[:, None] + peer_rows) // devices, balanced_rows
    ).astype(jnp.int32)
    landed = jnp.zeros((balanced_rows, local_width), attended.dtype)
    moved_rows = landed.at[incoming_slots.reshape(-1)].set(
        incoming.reshape(-1, local_width), mode="drop"
    )
    partial_value = jnp.dot(
        moved_rows,
        lax.all_gather(out_weight, "pairs", axis=1, tiled=True),
        preferred_element_type=jnp.float32,
    )
    tensor_place = lax.axis_index("tensor")
    groups = partial_value.astype(jnp.bfloat16).reshape(balanced_rows, 4, local_width)
    first_partner = tensor_place + 1 - 2 * (tensor_place % 2)
    second_partner = 3 - tensor_place

    def pick(group):
        return lax.dynamic_index_in_dim(groups, group, 1, False)

    sent = jnp.stack([pick(first_partner), pick(3 - first_partner)])
    came = lax.ppermute(sent, "tensor", [(0, 1), (1, 0), (2, 3), (3, 2)])
    kept = jnp.stack([pick(tensor_place), pick(second_partner)])
    pair_sums = kept.astype(jnp.float32) + came.astype(jnp.float32)
    other_pair = lax.ppermute(pair_sums[1], "tensor", [(0, 3), (3, 0), (1, 2), (2, 1)])
    projected = (pair_sums[0] + other_pair).astype(jnp.bfloat16)
    return (residual.astype(jnp.float32) + projected.astype(jnp.float32)).astype(jnp.bfloat16)


def solution(mesh):
    in_specs = (
        P("pairs", "tensor"),
        P("pairs", "tensor"),
        P("pairs", "tensor"),
        P("pairs"),
        P("tensor", "pairs"),
        P("pairs", "tensor"),
    )
    out_specs = P("pairs", "tensor")
    return jax.shard_map(shards, mesh=mesh, in_specs=in_specs, out_specs=out_specs, check_vma=False)
```

```python
import jax
import jax.numpy as jnp
from jax import lax
from jax.sharding import PartitionSpec as P

HEAD = 64
SLOTS = 8


def carried_in(part, axis):
    place = lax.axis_index(axis)
    gathered = lax.all_gather(part, axis)
    earlier = jnp.arange(gathered.shape[0], dtype=jnp.int32) < place
    return jnp.sum(jnp.where(earlier, gathered, 0)), gathered


def attend_group(query_part, key_part, value_part, allowed):
    scores = jnp.einsum("qhd,khd->hqk", query_part, key_part, preferred_element_type=jnp.float32)
    masked = jnp.where(allowed[None], scores, -1e30)
    row_top = jnp.max(masked, axis=2, keepdims=True)
    exp_terms = jnp.where(allowed[None], jnp.exp(masked - row_top), 0.0)
    row_total = jnp.maximum(jnp.sum(exp_terms, axis=2, keepdims=True), 1.0)
    weights = (exp_terms / row_total).astype(jnp.bfloat16)
    mixed = jnp.einsum("hqk,khd->qhd", weights, value_part, preferred_element_type=jnp.float32)
    return mixed.astype(jnp.bfloat16)


def shards(queries, key_rows, value_rows, pair_ids, out_weight, residual):
    cap_rows = queries.shape[0]
    local_width = queries.shape[1]
    heads_local = local_width // HEAD
    group_size = 4
    balanced_rows = residual.shape[0]
    allowed = (pair_ids[:, None] == pair_ids[None, :]) & (pair_ids[:, None] < SLOTS)

    def split_heads(stacked):
        return stacked.reshape(cap_rows, heads_local // group_size, group_size, HEAD).transpose(
            1, 0, 2, 3
        )

    def per_group(operands):
        return attend_group(operands[0], operands[1], operands[2], allowed)

    grouped = lax.map(
        per_group, (split_heads(queries), split_heads(key_rows), split_heads(value_rows))
    )
    attended = grouped.transpose(1, 0, 2, 3).reshape(cap_rows, local_width)
    live_rows = jnp.sum((pair_ids < SLOTS).astype(jnp.int32))
    devices = lax.axis_size("pairs")
    row_start, all_live = carried_in(live_rows, "pairs")
    all_start = jnp.cumsum(all_live) - all_live
    per_peer = cap_rows // devices
    peer_index = jnp.arange(devices, dtype=jnp.int32)
    turn_index = jnp.arange(per_peer, dtype=jnp.int32)
    source_rows = ((peer_index - row_start) % devices)[:, None] + devices * turn_index[None, :]
    outgoing = jnp.take(attended, source_rows.reshape(-1), axis=0).reshape(
        devices, per_peer, local_width
    )
    incoming = lax.all_to_all(outgoing, "pairs", split_axis=0, concat_axis=0, tiled=True)
    me = lax.axis_index("pairs")
    peer_rows = ((me - all_start) % devices)[:, None] + devices * turn_index[None, :]
    incoming_slots = jnp.where(
        peer_rows < all_live[:, None], (all_start[:, None] + peer_rows) // devices, balanced_rows
    ).astype(jnp.int32)
    landed = jnp.zeros((balanced_rows, local_width), attended.dtype)
    moved_rows = landed.at[incoming_slots.reshape(-1)].set(
        incoming.reshape(-1, local_width), mode="drop"
    )
    partial_value = jnp.dot(
        moved_rows,
        lax.all_gather(out_weight, "pairs", axis=1, tiled=True),
        preferred_element_type=jnp.float32,
    )
    tensor_parts = lax.axis_size("tensor")
    by_group = (
        partial_value.astype(jnp.bfloat16)
        .reshape(balanced_rows, tensor_parts, local_width)
        .transpose(1, 0, 2)
    )
    received = lax.all_to_all(by_group, "tensor", 0, 0, tiled=True)
    total = received[0].astype(jnp.float32)
    for group in range(1, tensor_parts):
        total = total + received[group].astype(jnp.float32)
    projected = total.astype(jnp.bfloat16)
    return (residual.astype(jnp.float32) + projected.astype(jnp.float32)).astype(jnp.bfloat16)


def solution(mesh):
    in_specs = (
        P("pairs", "tensor"),
        P("pairs", "tensor"),
        P("pairs", "tensor"),
        P("pairs"),
        P("tensor", "pairs"),
        P("pairs", "tensor"),
    )
    out_specs = P("pairs", "tensor")
    return jax.shard_map(shards, mesh=mesh, in_specs=in_specs, out_specs=out_specs, check_vma=False)
```

```python
import jax
import jax.numpy as jnp
from jax import lax
from jax.sharding import PartitionSpec as P

HEAD = 64
SLOTS = 8


def carried_in(part, axis):
    place = lax.axis_index(axis)
    gathered = lax.all_gather(part, axis)
    earlier = jnp.arange(gathered.shape[0], dtype=jnp.int32) < place
    return jnp.sum(jnp.where(earlier, gathered, 0)), gathered


def attend_group(query_part, key_part, value_part, allowed):
    scores = jnp.einsum("qhd,khd->hqk", query_part, key_part, preferred_element_type=jnp.float32)
    masked = jnp.where(allowed[None], scores, -1e30)
    row_top = jnp.max(masked, axis=2, keepdims=True)
    exp_terms = jnp.where(allowed[None], jnp.exp(masked - row_top), 0.0)
    row_total = jnp.maximum(jnp.sum(exp_terms, axis=2, keepdims=True), 1.0)
    weights = (exp_terms / row_total).astype(jnp.bfloat16)
    mixed = jnp.einsum("hqk,khd->qhd", weights, value_part, preferred_element_type=jnp.float32)
    return mixed.astype(jnp.bfloat16)


def shards(queries, key_rows, value_rows, pair_ids, out_weight, residual):
    cap_rows = queries.shape[0]
    local_width = queries.shape[1]
    heads_local = local_width // HEAD
    group_size = 4
    balanced_rows = residual.shape[0]
    allowed = (pair_ids[:, None] == pair_ids[None, :]) & (pair_ids[:, None] < SLOTS)

    def split_heads(stacked):
        return stacked.reshape(cap_rows, heads_local // group_size, group_size, HEAD).transpose(
            1, 0, 2, 3
        )

    def per_group(operands):
        return attend_group(operands[0], operands[1], operands[2], allowed)

    grouped = lax.map(
        per_group, (split_heads(queries), split_heads(key_rows), split_heads(value_rows))
    )
    attended = grouped.transpose(1, 0, 2, 3).reshape(cap_rows, local_width)
    live_rows = jnp.sum((pair_ids < SLOTS).astype(jnp.int32))
    devices = lax.axis_size("pairs")
    row_start, all_live = carried_in(live_rows, "pairs")
    all_start = jnp.cumsum(all_live) - all_live
    per_peer = cap_rows // devices
    peer_index = jnp.arange(devices, dtype=jnp.int32)
    turn_index = jnp.arange(per_peer, dtype=jnp.int32)
    source_rows = ((peer_index - row_start) % devices)[:, None] + devices * turn_index[None, :]
    outgoing = jnp.take(attended, source_rows.reshape(-1), axis=0).reshape(
        devices, per_peer, local_width
    )
    incoming = lax.all_to_all(outgoing, "pairs", split_axis=0, concat_axis=0, tiled=True)
    me = lax.axis_index("pairs")
    peer_rows = ((me - all_start) % devices)[:, None] + devices * turn_index[None, :]
    incoming_slots = jnp.where(
        peer_rows < all_live[:, None], (all_start[:, None] + peer_rows) // devices, balanced_rows
    ).astype(jnp.int32)
    landed = jnp.zeros((balanced_rows, local_width), attended.dtype)
    moved_rows = landed.at[incoming_slots.reshape(-1)].set(
        incoming.reshape(-1, local_width), mode="drop"
    )
    tensor_parts = lax.axis_size("tensor")
    group_weight = lax.all_gather(out_weight, "pairs", axis=1, tiled=True)
    by_group = jnp.einsum(
        "rk,kgn->grn",
        moved_rows,
        group_weight.reshape(local_width, tensor_parts, local_width),
        preferred_element_type=jnp.float32,
    ).astype(jnp.bfloat16)
    received = lax.all_to_all(by_group, "tensor", 0, 0, tiled=True)
    projected = jnp.sum(received.astype(jnp.float32), axis=0).astype(jnp.bfloat16)
    return (residual.astype(jnp.float32) + projected.astype(jnp.float32)).astype(jnp.bfloat16)


def solution(mesh):
    in_specs = (
        P("pairs", "tensor"),
        P("pairs", "tensor"),
        P("pairs", "tensor"),
        P("pairs"),
        P("tensor", "pairs"),
        P("pairs", "tensor"),
    )
    out_specs = P("pairs", "tensor")
    return jax.shard_map(shards, mesh=mesh, in_specs=in_specs, out_specs=out_specs, check_vma=False)
```
